512 devices in a mesh: gx: 8 (over y_hi, core), gy: 16 (over y_lo, z), gz: 4 (over x).
Axes of the slice: x: 4, y: 8 (y_hi: 4, y_lo: 2; y = y_hi * 2 + y_lo), z: 8, core: 2. Of those that a mesh axis runs over, the one named last changes fastest.
Arguments:
- views: float32 [6, 64, 256, 512], P(None, 'gx', ('gy', 'gz')), may hold values from 0.2 to 5
- estimate: float32 [64, 256, 512], P('gx', 'gy', 'gz'), may hold values from 0.5 to 2
- psf: float32 [6, 3, 17], replicated, may hold values from 0.2 to 1
- extents: int32 [6, 3, 2], replicated, may hold values from 0 to 512, as said below
Outputs:
- deconvolved: float32 [64, 256, 512], P('gx', 'gy', 'gz')
The draws below stay inside these ranges and needn't reach their ends.
Inputs may be any that keep to these rules, and one draw needn't show every extreme that they name: extents[v, a, 0] < extents[v, a, 1] <= the number of cells along axis a (64, 256, 512 for a = 0, 1, 2).
All inputs are finite; a program needn't handle non-finite values.
Results may differ from the reference program's by a relative error of at most 0.0003.
Values sent between devices are 32-bit elements; how exact they have to be, the bound alone decides.
No kernel may reach another device: no remote copies, remote signals or barrier semaphores. Data moves between devices by JAX's collectives and lax.ppermute only.
A program may use at most 64 MiB of HBM per device.

```python
import math
import jax
import jax.numpy as jnp
from jax import lax

V = 6
H = 8
K = 17
ITERS = 2
NX = 64
NY = 256
NZ = 512


def draw_extents(key, part):
    first_key, second_key = jax.random.split(jax.random.fold_in(key, 17))
    cells = jnp.array([NX, NY, NZ], jnp.int32)[None, :]
    half = cells // 2
    lower_bits = jax.random.randint(first_key, (V, 3), 0, 1 << 20)
    upper_bits = jax.random.randint(second_key, (V, 3), 0, 1 << 20)
    low = lower_bits % half
    high_even = half + 1 + upper_bits % (cells - half)
    odd_view = (jnp.arange(V, dtype=jnp.int32) % 2 == 1)[:, None]
    lower = jnp.where(odd_view, low, jnp.zeros_like(low))
    upper = jnp.where(odd_view, jnp.broadcast_to(cells, (V, 3)), high_even)
    return jnp.stack([lower, upper], axis=-1).astype(jnp.int32)


def block_levels(own_key, dims, cuts, smallest, high):
    def one(axis_at, parts):
        heights = jax.random.uniform(jax.random.fold_in(jax.random.fold_in(own_key, 6), axis_at), (parts,), jnp.float32, smallest / len(cuts), high / len(cuts))
        return jnp.repeat(jnp.exp(heights), dims[axis_at] // parts).reshape((-1,) + (1,) * (len(dims) - axis_at - 1))

    gain = one(*cuts[0])
    for cut in cuts[1:]:
        gain = gain * one(*cut)
    return gain


def setup_inputs(seed: int = 0) -> dict:
    seeds = jax.random.split(jax.random.key(seed), 5)
    views = jnp.clip(jnp.exp(math.log(5.0) - 3.218876 * jax.random.uniform(seeds[0], (V, NX, NY, NZ), jnp.float32) ** block_levels(seeds[0], (V, NX, NY, NZ), ((1, 8), (2, 64)), -0.2, 0.2)), 0.2, 5.0)
    estimate = jnp.clip(jnp.exp(math.log(2.0) - 1.3862944 * jax.random.uniform(seeds[1], (NX, NY, NZ), jnp.float32) ** block_levels(seeds[1], (NX, NY, NZ), ((0, 8), (1, 16), (2, 4)), -0.2, 0.2)), 0.5, 2.0)
    psf = jnp.clip(jnp.exp(jax.random.uniform(seeds[2], (V, 3, K), jnp.float32, math.log(0.2), math.log(1.0))), 0.2, 1.0)
    extents = draw_extents(jax.random.fold_in(seeds[4], 71), 0)
    return dict(views=views, estimate=estimate, psf=psf, extents=extents)


def blur_axis(volume, kernel, axis):
    length = volume.shape[axis]
    widths = [(0, 0), (0, 0), (0, 0)]
    widths[axis] = (H, H)
    padded = jnp.pad(volume, widths)
    total = kernel[0] * lax.slice_in_dim(padded, 0, length, axis=axis)
    for tap in range(1, K):
        total = total + kernel[tap] * lax.slice_in_dim(padded, tap, tap + length, axis=axis)
    return total


def blur_three(volume, kernels):
    for axis in range(3):
        volume = blur_axis(volume, kernels[axis], axis)
    return volume


def weight_of(bounds):
    first = jnp.arange(NX, dtype=jnp.int32)[:, None, None]
    second = jnp.arange(NY, dtype=jnp.int32)[None, :, None]
    third = jnp.arange(NZ, dtype=jnp.int32)[None, None, :]
    inside = (first >= bounds[0, 0]) & (first < bounds[0, 1])
    inside = inside & (second >= bounds[1, 0]) & (second < bounds[1, 1])
    inside = inside & (third >= bounds[2, 0]) & (third < bounds[2, 1])
    return jnp.where(inside, jnp.float32(1.0), jnp.float32(0.25))


def reference(views, estimate, psf, extents):
    taps = psf / jnp.sum(psf, axis=-1, keepdims=True)
    flipped = taps[:, :, ::-1]
    deconvolved = estimate

    for step in range(ITERS):
        def one_view(carry, inputs):
            image, kernels, back_kernels, bounds = inputs
            blurred = blur_three(deconvolved, kernels)
            ratio = image / blurred
            back = blur_three(ratio, back_kernels)
            weight = weight_of(bounds)
            return (carry[0] + weight * back, carry[1] + weight), None

        start = (jnp.zeros((NX, NY, NZ), jnp.float32), jnp.zeros((NX, NY, NZ), jnp.float32))
        (summed, weight_sum), unused = lax.scan(one_view, start, (views, taps, flipped, extents))
        deconvolved = deconvolved * (summed / weight_sum)
    return deconvolved
```

```python
import jax
import jax.numpy as jnp
from jax import lax
from jax.sharding import PartitionSpec as P

H = 8
K = 17
ITERS = 2


def padded(array, sides):
    for axis, dim, width in sides:
        devices, length = (lax.axis_size(axis), array.shape[dim])
        hops = -(-width // length)
        befores, afters = [], []
        for k in range(1, hops + 1):
            part = min(length, width - (k - 1) * length)
            up = [(i, i + k) for i in range(devices - k)]
            down = [(j, i) for i, j in up]
            last = lax.slice_in_dim(array, length - part, length, axis=dim)
            leading = lax.slice_in_dim(array, 0, part, axis=dim)
            befores.insert(0, lax.ppermute(last, axis, up))
            afters.append(lax.ppermute(leading, axis, down))
        array = jnp.concatenate(befores + [array] + afters, axis=dim)
    return array


def band_matrix(kernels, length):
    rows = length + 2 * H
    offset = (
        jnp.arange(rows, dtype=jnp.int32)[:, None] - jnp.arange(length, dtype=jnp.int32)[None, :]
    )
    picks = (offset[:, :, None] == jnp.arange(K, dtype=jnp.int32)[None, None, :]).astype(
        jnp.float32
    )
    return jnp.einsum("ijt,vt->vij", picks, kernels, precision=lax.Precision.HIGHEST)


def blur_along(padded, kernels, axis, length):
    matrix = band_matrix(kernels, length)
    source = "vxyz" if padded.shape[0] == kernels.shape[0] else "uxyz"
    letter = "vxyz"[axis]
    target = "vxyz".replace(letter, "a")
    form = source + ",v" + letter + "a->" + target
    return jnp.einsum(form, padded, matrix, precision=lax.Precision.HIGHEST)


def blur_padded(padded, kernels, sides):
    result = padded
    for axis in range(3):
        result = blur_along(result, kernels[:, axis], axis + 1, sides[axis])
    return result


def positions(sides, margin):
    names = ("gx", "gy", "gz")
    return [
        lax.axis_index(names[a]) * sides[a] - margin + jnp.arange(sides[a] + 2 * margin, dtype=jnp.int32)
        for a in range(3)
    ]


def view_weights(extents, sides):
    first, second, third = positions(sides, 0)
    inside_first = (first[None, :] >= extents[:, 0, 0:1]) & (first[None, :] < extents[:, 0, 1:2])
    inside_second = (second[None, :] >= extents[:, 1, 0:1]) & (second[None, :] < extents[:, 1, 1:2])
    inside_third = (third[None, :] >= extents[:, 2, 0:1]) & (third[None, :] < extents[:, 2, 1:2])
    inside = (
        inside_first[:, :, None, None]
        & inside_second[:, None, :, None]
        & inside_third[:, None, None, :]
    )
    return jnp.where(inside, jnp.float32(1.0), jnp.float32(0.25))


def grid_mask(sides, totals):
    first, second, third = positions(sides, H)
    inside = [(p >= 0) & (p < n) for p, n in zip((first, second, third), totals)]
    return inside[0][:, None, None] & inside[1][None, :, None] & inside[2][None, None, :]


def shards(views, estimate, psf, extents):
    images = lax.all_to_all(views, "gz", split_axis=3, concat_axis=2, tiled=True)
    sides = estimate.shape
    totals = tuple(s * lax.axis_size(n) for s, n in zip(sides, ("gx", "gy", "gz")))
    wide = tuple(s + 2 * H for s in sides)
    images = padded(images, (("gx", 1, H), ("gy", 2, H), ("gz", 3, H)))
    inside = grid_mask(sides, totals)[None]
    taps = psf / jnp.sum(psf, axis=-1, keepdims=True)
    flipped = taps[:, :, ::-1]
    weights = view_weights(extents, sides)
    weight_sum = jnp.sum(weights, axis=0)
    deconvolved = estimate
    for step in range(ITERS):
        halo = padded(deconvolved, (("gx", 0, 2 * H), ("gy", 1, 2 * H), ("gz", 2, 2 * H)))
        blurred = blur_padded(halo[None], taps, wide)
        ratio = jnp.where(inside, images / blurred, jnp.float32(0.0))
        back = blur_padded(ratio, flipped, sides)
        summed = jnp.sum(weights * back, axis=0)
        deconvolved = deconvolved * (summed / weight_sum)
    return deconvolved


def solution(mesh):
    placed = (P(None, "gx", ("gy", "gz"), None), P("gx", "gy", "gz"), P(), P())
    return jax.shard_map(
        shards, mesh=mesh, in_specs=placed, out_specs=P("gx", "gy", "gz"), check_vma=False
    )
```

```python
import jax
import jax.numpy as jnp
from jax import lax
from jax.sharding import PartitionSpec as P

H = 8
K = 17
ITERS = 2


def padded(array, sides):
    for axis, dim, width in sides:
        devices, length = (lax.axis_size(axis), array.shape[dim])
        hops = -(-width // length)
        befores, afters = [], []
        for k in range(1, hops + 1):
            part = min(length, width - (k - 1) * length)
            up = [(i, i + k) for i in range(devices - k)]
            down = [(j, i) for i, j in up]
            last = lax.slice_in_dim(array, length - part, length, axis=dim)
            leading = lax.slice_in_dim(array, 0, part, axis=dim)
            befores.insert(0, lax.ppermute(last, axis, up))
            afters.append(lax.ppermute(leading, axis, down))
        array = jnp.concatenate(befores + [array] + afters, axis=dim)
    return array


def band_matrix(kernels, length):
    rows = length + 2 * H
    count = kernels.shape[0]
    column = jnp.pad(kernels, ((0, 0), (0, rows + 1 - K)))
    tiled = jnp.tile(column, (1, length))[:, : length * rows]
    return jnp.swapaxes(tiled.reshape(count, length, rows), 1, 2)


def blur_along(padded, kernels, axis, length):
    matrix = band_matrix(kernels, length)
    source = "vxyz" if padded.shape[0] == kernels.shape[0] else "uxyz"
    letter = "vxyz"[axis]
    target = "vxyz".replace(letter, "a")
    form = source + ",v" + letter + "a->" + target
    return jnp.einsum(form, padded, matrix, precision=lax.Precision.HIGH)


def blur_padded(padded, kernels, sides):
    result = padded
    for axis in range(3):
        result = blur_along(result, kernels[:, axis], axis + 1, sides[axis])
    return result


def positions(sides, margin):
    names = ("gx", "gy", "gz")
    return [
        lax.axis_index(names[a]) * sides[a] - margin + jnp.arange(sides[a] + 2 * margin, dtype=jnp.int32)
        for a in range(3)
    ]


def view_weights(extents, sides):
    first, second, third = positions(sides, 0)
    inside_first = (first[None, :] >= extents[:, 0, 0:1]) & (first[None, :] < extents[:, 0, 1:2])
    inside_second = (second[None, :] >= extents[:, 1, 0:1]) & (second[None, :] < extents[:, 1, 1:2])
    inside_third = (third[None, :] >= extents[:, 2, 0:1]) & (third[None, :] < extents[:, 2, 1:2])
    inside = (
        inside_first[:, :, None, None]
        & inside_second[:, None, :, None]
        & inside_third[:, None, None, :]
    )
    return jnp.where(inside, jnp.float32(1.0), jnp.float32(0.25))


def grid_mask(sides, totals):
    first, second, third = positions(sides, H)
    inside = [(p >= 0) & (p < n) for p, n in zip((first, second, third), totals)]
    return inside[0][:, None, None] & inside[1][None, :, None] & inside[2][None, None, :]


def redistribute(views, axis):
    devices = lax.axis_size(axis)
    me = lax.axis_index(axis)
    rows = views.shape[2]
    width = views.shape[3] // devices
    images = jnp.zeros(views.shape[:2] + (rows * devices, width), views.dtype)
    for shift in range(devices):
        chunk = lax.dynamic_slice_in_dim(views, ((me + shift) % devices) * width, width, axis=3)
        if shift:
            pairs = [(i, (i + shift) % devices) for i in range(devices)]
            chunk = lax.ppermute(chunk, axis, pairs)
        start = ((me - shift) % devices) * rows
        images = lax.dynamic_update_slice_in_dim(images, chunk, start, axis=2)
    return images


def shards(views, estimate, psf, extents):
    images = redistribute(views, "gz")
    sides = estimate.shape
    totals = tuple(s * lax.axis_size(n) for s, n in zip(sides, ("gx", "gy", "gz")))
    wide = tuple(s + 2 * H for s in sides)
    images = padded(images, (("gx", 1, H), ("gy", 2, H), ("gz", 3, H)))
    inside = grid_mask(sides, totals)[None]
    taps = psf / jnp.sum(psf, axis=-1, keepdims=True)
    flipped = taps[:, :, ::-1]
    weights = view_weights(extents, sides)
    weight_sum = jnp.sum(weights, axis=0)
    deconvolved = estimate
    for step in range(ITERS):
        halo = padded(deconvolved, (("gx", 0, 2 * H), ("gy", 1, 2 * H), ("gz", 2, 2 * H)))
        blurred = blur_padded(halo[None], taps, wide)
        ratio = jnp.where(inside, images / blurred, jnp.float32(0.0))
        back = blur_padded(ratio, flipped, sides)
        summed = jnp.sum(weights * back, axis=0)
        deconvolved = deconvolved * (summed / weight_sum)
    return deconvolved


def solution(mesh):
    placed = (P(None, "gx", ("gy", "gz"), None), P("gx", "gy", "gz"), P(), P())
    return jax.shard_map(
        shards, mesh=mesh, in_specs=placed, out_specs=P("gx", "gy", "gz"), check_vma=False
    )
```

```python
import itertools

import jax
import jax.numpy as jnp
from jax import lax
from jax.sharding import PartitionSpec as P

H = 8
K = 17
ITERS = 2


def padded(array, sides):
    for axis, dim, width in sides:
        devices, length = (lax.axis_size(axis), array.shape[dim])
        hops = -(-width // length)
        befores, afters = [], []
        for k in range(1, hops + 1):
            part = min(length, width - (k - 1) * length)
            up = [(i, i + k) for i in range(devices - k)]
            down = [(j, i) for i, j in up]
            last = lax.slice_in_dim(array, length - part, length, axis=dim)
            leading = lax.slice_in_dim(array, 0, part, axis=dim)
            befores.insert(0, lax.ppermute(last, axis, up))
            afters.append(lax.ppermute(leading, axis, down))
        array = jnp.concatenate(befores + [array] + afters, axis=dim)
    return array


def joint(array, sides):
    names = tuple(axis for axis, dim, width in sides)
    sizes = [lax.axis_size(axis) for axis in names]
    options = []
    for axis, dim, width in sides:
        length = array.shape[dim]
        hops = -(-width // length)
        options.append([(k, min(length, width - (abs(k) - 1) * length)) for k in range(-hops, hops + 1)])
    pieces = {}
    for combo in itertools.product(*options):
        offsets = tuple(k for k, part in combo)
        piece = array
        for (axis, dim, width), (k, part) in zip(sides, combo):
            length = array.shape[dim]
            if k < 0:
                piece = lax.slice_in_dim(piece, length - part, length, axis=dim)
            elif k > 0:
                piece = lax.slice_in_dim(piece, 0, part, axis=dim)
        if any(offsets):
            pairs = []
            for index in itertools.product(*[range(n) for n in sizes]):
                source = tuple(i + k for i, k in zip(index, offsets))
                if all(0 <= i < n for i, n in zip(source, sizes)):
                    pairs.append((linear(source, sizes), linear(index, sizes)))
            piece = lax.ppermute(piece, names, pairs)
        pieces[offsets] = piece
    return assemble(pieces, [[k for k, part in option] for option in options], [dim for axis, dim, width in sides])


def linear(index, sizes):
    value = 0
    for i, n in zip(index, sizes):
        value = value * n + i
    return value


def assemble(pieces, choices, dims, prefix=()):
    if len(prefix) == len(choices):
        return pieces[prefix]
    parts = [assemble(pieces, choices, dims, prefix + (k,)) for k in choices[len(prefix)]]
    return jnp.concatenate(parts, axis=dims[len(prefix)])


def band_matrix(kernels, length):
    rows = length + 2 * H
    count = kernels.shape[0]
    column = jnp.pad(kernels, ((0, 0), (0, rows + 1 - K)))
    tiled = jnp.tile(column, (1, length))[:, : length * rows]
    return jnp.swapaxes(tiled.reshape(count, length, rows), 1, 2)


def blur_along(padded, kernels, axis, length):
    matrix = band_matrix(kernels, length)
    source = "vxyz" if padded.shape[0] == kernels.shape[0] else "uxyz"
    letter = "vxyz"[axis]
    target = "vxyz".replace(letter, "a")
    form = source + ",v" + letter + "a->" + target
    return jnp.einsum(form, padded, matrix, precision=lax.Precision.HIGH)


def blur_padded(padded, kernels, sides):
    result = padded
    for axis in range(3):
        result = blur_along(result, kernels[:, axis], axis + 1, sides[axis])
    return result


def positions(sides, margin):
    names = ("gx", "gy", "gz")
    return [
        lax.axis_index(names[a]) * sides[a] - margin + jnp.arange(sides[a] + 2 * margin, dtype=jnp.int32)
        for a in range(3)
    ]


def view_weights(extents, sides):
    first, second, third = positions(sides, 0)
    inside_first = (first[None, :] >= extents[:, 0, 0:1]) & (first[None, :] < extents[:, 0, 1:2])
    inside_second = (second[None, :] >= extents[:, 1, 0:1]) & (second[None, :] < extents[:, 1, 1:2])
    inside_third = (third[None, :] >= extents[:, 2, 0:1]) & (third[None, :] < extents[:, 2, 1:2])
    inside = (
        inside_first[:, :, None, None]
        & inside_second[:, None, :, None]
        & inside_third[:, None, None, :]
    )
    return jnp.where(inside, jnp.float32(1.0), jnp.float32(0.25))


def grid_mask(sides, totals):
    first, second, third = positions(sides, H)
    inside = [(p >= 0) & (p < n) for p, n in zip((first, second, third), totals)]
    return inside[0][:, None, None] & inside[1][None, :, None] & inside[2][None, None, :]


def redistribute(views, axis):
    devices = lax.axis_size(axis)
    me = lax.axis_index(axis)
    rows = views.shape[2]
    width = views.shape[3] // devices
    images = jnp.zeros(views.shape[:2] + (rows * devices, width), views.dtype)
    for shift in range(devices):
        chunk = lax.dynamic_slice_in_dim(views, ((me + shift) % devices) * width, width, axis=3)
        if shift:
            pairs = [(i, (i + shift) % devices) for i in range(devices)]
            chunk = lax.ppermute(chunk, axis, pairs)
        start = ((me - shift) % devices) * rows
        images = lax.dynamic_update_slice_in_dim(images, chunk, start, axis=2)
    return images


def shards(views, estimate, psf, extents):
    images = redistribute(views, "gz")
    sides = estimate.shape
    totals = tuple(s * lax.axis_size(n) for s, n in zip(sides, ("gx", "gy", "gz")))
    wide = tuple(s + 2 * H for s in sides)
    images = padded(joint(images, (("gx", 1, H), ("gy", 2, H))), (("gz", 3, H),))
    inside = grid_mask(sides, totals)[None]
    taps = psf / jnp.sum(psf, axis=-1, keepdims=True)
    flipped = taps[:, :, ::-1]
    weights = view_weights(extents, sides)
    weight_sum = jnp.sum(weights, axis=0)
    deconvolved = estimate
    for step in range(ITERS):
        halo = joint(deconvolved, (("gx", 0, 2 * H), ("gy", 1, 2 * H)))
        halo = padded(halo, (("gz", 2, 2 * H),))
        blurred = blur_padded(halo[None], taps, wide)
        ratio = jnp.where(inside, images / blurred, jnp.float32(0.0))
        back = blur_padded(ratio, flipped, sides)
        summed = jnp.sum(weights * back, axis=0)
        deconvolved = deconvolved * (summed / weight_sum)
    return deconvolved


def solution(mesh):
    placed = (P(None, "gx", ("gy", "gz"), None), P("gx", "gy", "gz"), P(), P())
    return jax.shard_map(
        shards, mesh=mesh, in_specs=placed, out_specs=P("gx", "gy", "gz"), check_vma=False
    )
```

```python
import jax
import jax.numpy as jnp
from jax import lax
from jax.sharding import PartitionSpec as P

H = 8
K = 17
ITERS = 2


def padded(array, sides):
    for axis, dim, width in sides:
        devices, length = (lax.axis_size(axis), array.shape[dim])
        hops = -(-width // length)
        befores, afters = [], []
        for k in range(1, hops + 1):
            part = min(length, width - (k - 1) * length)
            up = [(i, i + k) for i in range(devices - k)]
            down = [(j, i) for i, j in up]
            last = lax.slice_in_dim(array, length - part, length, axis=dim)
            leading = lax.slice_in_dim(array, 0, part, axis=dim)
            befores.insert(0, lax.ppermute(last, axis, up))
            afters.append(lax.ppermute(leading, axis, down))
        array = jnp.concatenate(befores + [array] + afters, axis=dim)
    return array


def band_matrix(kernels, length):
    rows = length + 2 * H
    count = kernels.shape[0]
    column = jnp.pad(kernels, ((0, 0), (0, rows + 1 - K)))
    tiled = jnp.tile(column, (1, length))[:, : length * rows]
    return jnp.swapaxes(tiled.reshape(count, length, rows), 1, 2)


def blur_along(padded, kernels, axis, length):
    matrix = band_matrix(kernels, length)
    source = "vxyz" if padded.shape[0] == kernels.shape[0] else "uxyz"
    letter = "vxyz"[axis]
    target = "vxyz".replace(letter, "a")
    form = source + ",v" + letter + "a->" + target
    return jnp.einsum(form, padded, matrix, precision=lax.Precision.HIGH)


def blur_padded(padded, kernels, sides):
    result = padded
    for axis in range(3):
        result = blur_along(result, kernels[:, axis], axis + 1, sides[axis])
    return result


def positions(sides, margin):
    names = ("gx", "gy", "gz")
    return [
        lax.axis_index(names[a]) * sides[a] - margin + jnp.arange(sides[a] + 2 * margin, dtype=jnp.int32)
        for a in range(3)
    ]


def view_weights(extents, sides):
    first, second, third = positions(sides, 0)
    inside_first = (first[None, :] >= extents[:, 0, 0:1]) & (first[None, :] < extents[:, 0, 1:2])
    inside_second = (second[None, :] >= extents[:, 1, 0:1]) & (second[None, :] < extents[:, 1, 1:2])
    inside_third = (third[None, :] >= extents[:, 2, 0:1]) & (third[None, :] < extents[:, 2, 1:2])
    inside = (
        inside_first[:, :, None, None]
        & inside_second[:, None, :, None]
        & inside_third[:, None, None, :]
    )
    return jnp.where(inside, jnp.float32(1.0), jnp.float32(0.25))


def grid_mask(sides, totals):
    first, second, third = positions(sides, H)
    inside = [(p >= 0) & (p < n) for p, n in zip((first, second, third), totals)]
    return inside[0][:, None, None] & inside[1][None, :, None] & inside[2][None, None, :]


def redistribute(views, axis):
    devices = lax.axis_size(axis)
    me = lax.axis_index(axis)
    rows = views.shape[2]
    width = views.shape[3] // devices
    images = jnp.zeros(views.shape[:2] + (rows * devices, width), views.dtype)
    for shift in range(devices):
        chunk = lax.dynamic_slice_in_dim(views, ((me + shift) % devices) * width, width, axis=3)
        if shift:
            pairs = [(i, (i + shift) % devices) for i in range(devices)]
            chunk = lax.ppermute(chunk, axis, pairs)
        start = ((me - shift) % devices) * rows
        images = lax.dynamic_update_slice_in_dim(images, chunk, start, axis=2)
    return images


def window(array, axis, dim, length, width):
    widths = [(0, 0)] * array.ndim
    widths[dim] = (width, width)
    wide = jnp.pad(array, widths)
    start = lax.axis_index(axis) * length
    return lax.dynamic_slice_in_dim(wide, start, length + 2 * width, axis=dim)


def shards(views, estimate, psf, extents):
    images = lax.all_gather(views, "gz", axis=2, tiled=True)
    sides = estimate.shape
    totals = tuple(s * lax.axis_size(n) for s, n in zip(sides, ("gx", "gy", "gz")))
    wide = tuple(s + 2 * H for s in sides)
    images = window(images, "gz", 3, sides[2], H)
    images = padded(images, (("gx", 1, H), ("gy", 2, H)))
    inside = grid_mask(sides, totals)[None]
    taps = psf / jnp.sum(psf, axis=-1, keepdims=True)
    flipped = taps[:, :, ::-1]
    weights = view_weights(extents, sides)
    weight_sum = jnp.sum(weights, axis=0)
    deconvolved = estimate
    for step in range(ITERS):
        halo = window(lax.all_gather(deconvolved, "gx", axis=0, tiled=True), "gx", 0, sides[0], 2 * H)
        halo = padded(halo, (("gy", 1, 2 * H), ("gz", 2, 2 * H)))
        blurred = blur_padded(halo[None], taps, wide)
        ratio = jnp.where(inside, images / blurred, jnp.float32(0.0))
        back = blur_padded(ratio, flipped, sides)
        summed = jnp.sum(weights * back, axis=0)
        deconvolved = deconvolved * (summed / weight_sum)
    return deconvolved


def solution(mesh):
    placed = (P(None, "gx", ("gy", "gz"), None), P("gx", "gy", "gz"), P(), P())
    return jax.shard_map(
        shards, mesh=mesh, in_specs=placed, out_specs=P("gx", "gy", "gz"), check_vma=False
    )
```

```python
import jax
import jax.numpy as jnp
from jax import lax
from jax.sharding import PartitionSpec as P

H = 8
K = 17
ITERS = 2


def padded(array, sides):
    for axis, dim, width in sides:
        devices, length = (lax.axis_size(axis), array.shape[dim])
        hops = -(-width // length)
        befores, afters = [], []
        for k in range(1, hops + 1):
            part = min(length, width - (k - 1) * length)
            up = [(i, i + k) for i in range(devices - k)]
            down = [(j, i) for i, j in up]
            last = lax.slice_in_dim(array, length - part, length, axis=dim)
            leading = lax.slice_in_dim(array, 0, part, axis=dim)
            befores.insert(0, lax.ppermute(last, axis, up))
            afters.append(lax.ppermute(leading, axis, down))
        array = jnp.concatenate(befores + [array] + afters, axis=dim)
    return array


def band_matrix(kernels, length):
    rows = length + 2 * H
    count = kernels.shape[0]
    column = jnp.pad(kernels, ((0, 0), (0, rows + 1 - K)))
    tiled = jnp.tile(column, (1, length))[:, : length * rows]
    return jnp.swapaxes(tiled.reshape(count, length, rows), 1, 2)


def blur_along(padded, kernels, axis, length):
    matrix = band_matrix(kernels, length)
    source = "vxyz" if padded.shape[0] == kernels.shape[0] else "uxyz"
    letter = "vxyz"[axis]
    target = "vxyz".replace(letter, "a")
    form = source + ",v" + letter + "a->" + target
    return jnp.einsum(form, padded, matrix, precision=lax.Precision.HIGH)


def blur_padded(padded, kernels, sides):
    result = padded
    for axis in range(3):
        result = blur_along(result, kernels[:, axis], axis + 1, sides[axis])
    return result


def positions(sides, margin):
    names = ("gx", "gy", "gz")
    return [
        lax.axis_index(names[a]) * sides[a] - margin + jnp.arange(sides[a] + 2 * margin, dtype=jnp.int32)
        for a in range(3)
    ]


def view_weights(extents, sides):
    first, second, third = positions(sides, 0)
    inside_first = (first[None, :] >= extents[:, 0, 0:1]) & (first[None, :] < extents[:, 0, 1:2])
    inside_second = (second[None, :] >= extents[:, 1, 0:1]) & (second[None, :] < extents[:, 1, 1:2])
    inside_third = (third[None, :] >= extents[:, 2, 0:1]) & (third[None, :] < extents[:, 2, 1:2])
    inside = (
        inside_first[:, :, None, None]
        & inside_second[:, None, :, None]
        & inside_third[:, None, None, :]
    )
    return jnp.where(inside, jnp.float32(1.0), jnp.float32(0.25))


def grid_mask(sides, totals):
    first, second, third = positions(sides, H)
    inside = [(p >= 0) & (p < n) for p, n in zip((first, second, third), totals)]
    return inside[0][:, None, None] & inside[1][None, :, None] & inside[2][None, None, :]


def redistribute(views, axis):
    devices = lax.axis_size(axis)
    me = lax.axis_index(axis)
    rows = views.shape[2]
    width = views.shape[3] // devices
    images = jnp.zeros(views.shape[:2] + (rows * devices, width), views.dtype)
    for shift in range(devices):
        chunk = lax.dynamic_slice_in_dim(views, ((me + shift) % devices) * width, width, axis=3)
        if shift:
            pairs = [(i, (i + shift) % devices) for i in range(devices)]
            chunk = lax.ppermute(chunk, axis, pairs)
        start = ((me - shift) % devices) * rows
        images = lax.dynamic_update_slice_in_dim(images, chunk, start, axis=2)
    return images


def shards(views, estimate, psf, extents):
    images = redistribute(views, "gz")
    sides = estimate.shape
    totals = tuple(s * lax.axis_size(n) for s, n in zip(sides, ("gx", "gy", "gz")))
    wide = tuple(s + 2 * H for s in sides)
    inside = grid_mask(sides, totals)[None]
    taps = psf / jnp.sum(psf, axis=-1, keepdims=True)
    flipped = taps[:, :, ::-1]
    weights = view_weights(extents, sides)
    weight_sum = jnp.sum(weights, axis=0)
    deconvolved = estimate
    for step in range(ITERS):
        halo = padded(deconvolved, (("gx", 0, 2 * H), ("gy", 1, 2 * H), ("gz", 2, 2 * H)))
        if step == 0:
            halo, images = lax.optimization_barrier((halo, images))
            images = padded(images, (("gx", 1, H), ("gy", 2, H), ("gz", 3, H)))
        blurred = blur_padded(halo[None], taps, wide)
        ratio = jnp.where(inside, images / blurred, jnp.float32(0.0))
        back = blur_padded(ratio, flipped, sides)
        summed = jnp.sum(weights * back, axis=0)
        deconvolved = deconvolved * (summed / weight_sum)
    return deconvolved


def solution(mesh):
    placed = (P(None, "gx", ("gy", "gz"), None), P("gx", "gy", "gz"), P(), P())
    return jax.shard_map(
        shards, mesh=mesh, in_specs=placed, out_specs=P("gx", "gy", "gz"), check_vma=False
    )
```

```python
import jax
import jax.numpy as jnp
from jax import lax
from jax.sharding import PartitionSpec as P

H = 8
K = 17
ITERS = 2


def axis_count(axis):
    names = axis if isinstance(axis, tuple) else (axis,)
    count = 1
    for name in names:
        count *= lax.axis_size(name)
    return count


def padded(array, sides):
    for axis, dim, width in sides:
        devices, length = (axis_count(axis), array.shape[dim])
        rank = list(range(devices))
        if isinstance(axis, tuple):
            inner = lax.axis_size(axis[0])
            rank = [(b % inner) * (devices // inner) + b // inner for b in range(devices)]
        up = [(rank[i], rank[i + 1]) for i in range(devices - 1)]
        down = [(j, i) for i, j in up]
        last = lax.slice_in_dim(array, length - width, length, axis=dim)
        leading = lax.slice_in_dim(array, 0, width, axis=dim)
        before = lax.ppermute(last, axis, up)
        after = lax.ppermute(leading, axis, down)
        array = jnp.concatenate([before, array, after], axis=dim)
    return array


def band_matrix(kernels, length):
    rows = length + 2 * H
    count = kernels.shape[0]
    column = jnp.pad(kernels, ((0, 0), (0, rows + 1 - K)))
    tiled = jnp.tile(column, (1, length))[:, : length * rows]
    return jnp.swapaxes(tiled.reshape(count, length, rows), 1, 2)


def blur_along(padded, kernels, axis, length):
    matrix = band_matrix(kernels, length)
    have = padded.shape[axis]
    low = (length + 2 * H - have) // 2
    matrix = matrix[:, low : low + have]
    source = "vxyz" if padded.shape[0] == kernels.shape[0] else "uxyz"
    letter = "vxyz"[axis]
    target = "vxyz".replace(letter, "a")
    form = source + ",v" + letter + "a->" + target
    return jnp.einsum(form, padded, matrix, precision=lax.Precision.HIGH)


def blur_padded(padded, kernels, sides):
    result = padded
    for axis in range(3):
        result = blur_along(result, kernels[:, axis], axis + 1, sides[axis])
    return result


def positions(sides, margin):
    block = lax.axis_index("gz") * lax.axis_size("gx") + lax.axis_index("gx")
    starts = (0, lax.axis_index("gy") * sides[1], block * sides[2])
    margins = (0, margin, margin)
    return [
        starts[a] - margins[a] + jnp.arange(sides[a] + 2 * margins[a], dtype=jnp.int32)
        for a in range(3)
    ]


def view_weights(extents, sides):
    first, second, third = positions(sides, 0)
    inside_first = (first[None, :] >= extents[:, 0, 0:1]) & (first[None, :] < extents[:, 0, 1:2])
    inside_second = (second[None, :] >= extents[:, 1, 0:1]) & (second[None, :] < extents[:, 1, 1:2])
    inside_third = (third[None, :] >= extents[:, 2, 0:1]) & (third[None, :] < extents[:, 2, 1:2])
    inside = (
        inside_first[:, :, None, None]
        & inside_second[:, None, :, None]
        & inside_third[:, None, None, :]
    )
    return jnp.where(inside, jnp.float32(1.0), jnp.float32(0.25))


def grid_mask(sides, totals):
    first, second, third = positions(sides, H)
    inside = [(p >= 0) & (p < n) for p, n in zip((first, second, third), totals)]
    return inside[0][:, None, None] & inside[1][None, :, None] & inside[2][None, None, :]


def gather_views(views, width):
    xs = lax.axis_size("gx")
    zs = lax.axis_size("gz")
    wide = jnp.pad(views, ((0, 0), (0, 0), (0, 0), (H, H)))
    windows = []
    for gx in range(xs):
        for gz in range(zs):
            start = (gz * xs + gx) * width
            windows.append(lax.slice_in_dim(wide, start, start + width + 2 * H, axis=3))
    sent = jnp.stack(windows)
    got = lax.all_to_all(sent, ("gx", "gz"), 0, 0, tiled=True)
    count, rows, span = views.shape[0], views.shape[2], width + 2 * H
    got = got.reshape(xs, zs, count, views.shape[1], rows, span)
    got = jnp.transpose(got, (2, 0, 3, 1, 4, 5))
    return got.reshape(count, xs * views.shape[1], zs * rows, span)


def shards(views, estimate, psf, extents):
    xs = lax.axis_size("gx")
    local = lax.all_to_all(estimate, "gx", 2, 0, tiled=True)
    sides = local.shape
    totals = (sides[0], sides[1] * lax.axis_size("gy"), sides[2] * xs * lax.axis_size("gz"))
    wide = (sides[0], sides[1] + 2 * H, sides[2] + 2 * H)
    images = gather_views(views, sides[2])
    images = padded(images, (("gy", 2, H),))
    inside = grid_mask(sides, totals)[None]
    taps = psf / jnp.sum(psf, axis=-1, keepdims=True)
    flipped = taps[:, :, ::-1]
    weights = view_weights(extents, sides)
    weight_sum = jnp.sum(weights, axis=0)
    deconvolved = local
    for step in range(ITERS):
        halo = padded(deconvolved, (("gy", 1, 2 * H), (("gx", "gz"), 2, 2 * H)))
        blurred = blur_padded(halo[None], taps, wide)
        ratio = jnp.where(inside, images / blurred, jnp.float32(0.0))
        back = blur_padded(ratio, flipped, sides)
        summed = jnp.sum(weights * back, axis=0)
        deconvolved = deconvolved * (summed / weight_sum)
    return lax.all_to_all(deconvolved, "gx", 0, 2, tiled=True)


def solution(mesh):
    placed = (P(None, "gx", ("gy", "gz"), None), P("gx", "gy", "gz"), P(), P())
    return jax.shard_map(
        shards, mesh=mesh, in_specs=placed, out_specs=P("gx", "gy", "gz"), check_vma=False
    )
```

```python
import jax
import jax.numpy as jnp
from jax import lax
from jax.sharding import PartitionSpec as P

H = 8
K = 17
ITERS = 2


def axis_count(axis):
    names = axis if isinstance(axis, tuple) else (axis,)
    count = 1
    for name in names:
        count *= lax.axis_size(name)
    return count


def padded(array, sides):
    for axis, dim, width in sides:
        devices, length = (axis_count(axis), array.shape[dim])
        rank = list(range(devices))
        if isinstance(axis, tuple):
            inner = lax.axis_size(axis[0])
            rank = [(b % inner) * (devices // inner) + b // inner for b in range(devices)]
        up = [(rank[i], rank[i + 1]) for i in range(devices - 1)]
        down = [(j, i) for i, j in up]
        last = lax.slice_in_dim(array, length - width, length, axis=dim)
        leading = lax.slice_in_dim(array, 0, width, axis=dim)
        before = lax.ppermute(last, axis, up)
        after = lax.ppermute(leading, axis, down)
        array = jnp.concatenate([before, array, after], axis=dim)
    return array


def band_matrix(kernels, length):
    rows = length + 2 * H
    count = kernels.shape[0]
    column = jnp.pad(kernels, ((0, 0), (0, rows + 1 - K)))
    tiled = jnp.tile(column, (1, length))[:, : length * rows]
    return jnp.swapaxes(tiled.reshape(count, length, rows), 1, 2)


def blur_along(padded, kernels, axis, length):
    matrix = band_matrix(kernels, length)
    have = padded.shape[axis]
    low = (length + 2 * H - have) // 2
    matrix = matrix[:, low : low + have]
    source = "vxyz" if padded.shape[0] == kernels.shape[0] else "uxyz"
    letter = "vxyz"[axis]
    target = "vxyz".replace(letter, "a")
    form = source + ",v" + letter + "a->" + target
    return jnp.einsum(form, padded, matrix, precision=lax.Precision.HIGH)


def blur_padded(padded, kernels, sides):
    result = padded
    for axis in range(3):
        result = blur_along(result, kernels[:, axis], axis + 1, sides[axis])
    return result


def positions(sides, margin):
    block = lax.axis_index("gz") * lax.axis_size("gx") + lax.axis_index("gx")
    starts = (0, lax.axis_index("gy") * sides[1], block * sides[2])
    margins = (0, margin, margin)
    return [
        starts[a] - margins[a] + jnp.arange(sides[a] + 2 * margins[a], dtype=jnp.int32)
        for a in range(3)
    ]


def view_weights(extents, sides):
    first, second, third = positions(sides, 0)
    inside_first = (first[None, :] >= extents[:, 0, 0:1]) & (first[None, :] < extents[:, 0, 1:2])
    inside_second = (second[None, :] >= extents[:, 1, 0:1]) & (second[None, :] < extents[:, 1, 1:2])
    inside_third = (third[None, :] >= extents[:, 2, 0:1]) & (third[None, :] < extents[:, 2, 1:2])
    inside = (
        inside_first[:, :, None, None]
        & inside_second[:, None, :, None]
        & inside_third[:, None, None, :]
    )
    return jnp.where(inside, jnp.float32(1.0), jnp.float32(0.25))


def grid_mask(sides, totals):
    first, second, third = positions(sides, H)
    inside = [(p >= 0) & (p < n) for p, n in zip((first, second, third), totals)]
    return inside[0][:, None, None] & inside[1][None, :, None] & inside[2][None, None, :]


def gather_views(views, width):
    xs = lax.axis_size("gx")
    zs = lax.axis_size("gz")
    wide = jnp.pad(views, ((0, 0), (0, 0), (0, 0), (H, H)))
    windows = []
    for gx in range(xs):
        for gz in range(zs):
            start = (gz * xs + gx) * width
            windows.append(lax.slice_in_dim(wide, start, start + width + 2 * H, axis=3))
    sent = jnp.stack(windows)
    got = lax.all_to_all(sent, ("gx", "gz"), 0, 0, tiled=True)
    count, rows, span = views.shape[0], views.shape[2], width + 2 * H
    got = got.reshape(xs, zs, count, views.shape[1], rows, span)
    got = jnp.transpose(got, (2, 0, 3, 1, 4, 5))
    return got.reshape(count, xs * views.shape[1], zs * rows, span)


def shards(views, estimate, psf, extents):
    xs = lax.axis_size("gx")
    local = lax.all_to_all(estimate, "gx", 2, 0, tiled=True)
    sides = local.shape
    totals = (sides[0], sides[1] * lax.axis_size("gy"), sides[2] * xs * lax.axis_size("gz"))
    wide = (sides[0], sides[1] + 2 * H, sides[2] + 2 * H)
    images = gather_views(views, sides[2])
    images = padded(images, (("gy", 2, H),))
    inside = grid_mask(sides, totals)[None]
    taps = psf / jnp.sum(psf, axis=-1, keepdims=True)
    flipped = taps[:, :, ::-1]
    weights = view_weights(extents, sides)
    weight_sum = jnp.sum(weights, axis=0)
    deconvolved = local
    for step in range(ITERS):
        halo = padded(deconvolved, (("gy", 1, 2 * H), (("gx", "gz"), 2, 2 * H)))
        blurred = blur_padded(halo[None], taps, wide)
        ratio = jnp.where(inside, images / blurred, jnp.float32(0.0))
        back = blur_padded(ratio, flipped, sides)
        summed = jnp.sum(weights * back, axis=0)
        deconvolved = deconvolved * (summed / weight_sum)
    return scatter_back(deconvolved, "gx")


def scatter_back(volume, axis):
    devices = lax.axis_size(axis)
    me = lax.axis_index(axis)
    rows = volume.shape[0] // devices
    width = volume.shape[2]
    result = jnp.zeros((rows, volume.shape[1], width * devices), volume.dtype)
    for shift in range(devices):
        chunk = lax.dynamic_slice_in_dim(volume, ((me + shift) % devices) * rows, rows, axis=0)
        if shift:
            pairs = [(i, (i + shift) % devices) for i in range(devices)]
            chunk = lax.ppermute(chunk, axis, pairs)
        start = ((me - shift) % devices) * width
        result = lax.dynamic_update_slice_in_dim(result, chunk, start, axis=2)
    return result


def solution(mesh):
    placed = (P(None, "gx", ("gy", "gz"), None), P("gx", "gy", "gz"), P(), P())
    return jax.shard_map(
        shards, mesh=mesh, in_specs=placed, out_specs=P("gx", "gy", "gz"), check_vma=False
    )
```

```python
import jax
import jax.numpy as jnp
from jax import lax
from jax.sharding import PartitionSpec as P

H = 8
K = 17
ITERS = 2


def axis_count(axis):
    names = axis if isinstance(axis, tuple) else (axis,)
    count = 1
    for name in names:
        count *= lax.axis_size(name)
    return count


def padded(array, sides):
    for axis, dim, width in sides:
        devices, length = (axis_count(axis), array.shape[dim])
        rank = list(range(devices))
        if isinstance(axis, tuple):
            inner = lax.axis_size(axis[0])
            rank = [(b % inner) * (devices // inner) + b // inner for b in range(devices)]
        up = [(rank[i], rank[i + 1]) for i in range(devices - 1)]
        down = [(j, i) for i, j in up]
        last = lax.slice_in_dim(array, length - width, length, axis=dim)
        leading = lax.slice_in_dim(array, 0, width, axis=dim)
        before = lax.ppermute(last, axis, up)
        after = lax.ppermute(leading, axis, down)
        array = jnp.concatenate([before, array, after], axis=dim)
    return array


def band_matrix(kernels, length):
    rows = length + 2 * H
    count = kernels.shape[0]
    column = jnp.pad(kernels, ((0, 0), (0, rows + 1 - K)))
    tiled = jnp.tile(column, (1, length))[:, : length * rows]
    return jnp.swapaxes(tiled.reshape(count, length, rows), 1, 2)


def blur_along(padded, kernels, axis, length):
    matrix = band_matrix(kernels, length)
    have = padded.shape[axis]
    low = (length + 2 * H - have) // 2
    matrix = matrix[:, low : low + have]
    source = "vxyz" if padded.shape[0] == kernels.shape[0] else "uxyz"
    letter = "vxyz"[axis]
    target = "vxyz".replace(letter, "a")
    form = source + ",v" + letter + "a->" + target
    return jnp.einsum(form, padded, matrix, precision=lax.Precision.HIGH)


def blur_padded(padded, kernels, sides):
    result = padded
    for axis in range(3):
        result = blur_along(result, kernels[:, axis], axis + 1, sides[axis])
    return result


def positions(sides, margin):
    block = lax.axis_index("gz") * lax.axis_size("gx") + lax.axis_index("gx")
    starts = (0, lax.axis_index("gy") * sides[1], block * sides[2])
    margins = (0, margin, margin)
    return [
        starts[a] - margins[a] + jnp.arange(sides[a] + 2 * margins[a], dtype=jnp.int32)
        for a in range(3)
    ]


def view_weights(extents, sides):
    first, second, third = positions(sides, 0)
    inside_first = (first[None, :] >= extents[:, 0, 0:1]) & (first[None, :] < extents[:, 0, 1:2])
    inside_second = (second[None, :] >= extents[:, 1, 0:1]) & (second[None, :] < extents[:, 1, 1:2])
    inside_third = (third[None, :] >= extents[:, 2, 0:1]) & (third[None, :] < extents[:, 2, 1:2])
    inside = (
        inside_first[:, :, None, None]
        & inside_second[:, None, :, None]
        & inside_third[:, None, None, :]
    )
    return jnp.where(inside, jnp.float32(1.0), jnp.float32(0.25))


def grid_mask(sides, totals):
    first, second, third = positions(sides, H)
    inside = [(p >= 0) & (p < n) for p, n in zip((first, second, third), totals)]
    return inside[0][:, None, None] & inside[1][None, :, None] & inside[2][None, None, :]


def gather_views(views, width):
    xs = lax.axis_size("gx")
    ys = lax.axis_size("gy")
    zs = lax.axis_size("gz")
    pairs = []
    for g in range(ys):
        for z in range(zs):
            target = g + 1 if 2 * z >= zs else g - 1
            if 0 <= target < ys:
                pairs.append((g * zs + z, target * zs + z))
    extra = lax.ppermute(views, ("gy", "gz"), pairs)
    both = jnp.concatenate([views, extra], axis=2)
    wide = jnp.pad(both, ((0, 0), (0, 0), (0, 0), (H, H)))
    windows = []
    for gx in range(xs):
        for gz in range(zs):
            start = (gz * xs + gx) * width
            windows.append(lax.slice_in_dim(wide, start, start + width + 2 * H, axis=3))
    sent = jnp.stack(windows)
    got = lax.all_to_all(sent, ("gx", "gz"), 0, 0, tiled=True)
    count, rows, span = views.shape[0], views.shape[2], width + 2 * H
    got = got.reshape(xs, zs, count, views.shape[1], 2, rows, span)
    half = zs // 2
    order = [(1, z) for z in range(half, zs)] + [(0, z) for z in range(zs)] + [(1, z) for z in range(half)]
    tiles = jnp.stack([got[:, z, :, :, kind] for kind, z in order], axis=3)
    tiles = jnp.transpose(tiles, (1, 0, 2, 3, 4, 5))
    return tiles.reshape(count, xs * views.shape[1], len(order) * rows, span)


def shards(views, estimate, psf, extents):
    xs = lax.axis_size("gx")
    local = lax.all_to_all(estimate, "gx", 2, 0, tiled=True)
    sides = local.shape
    totals = (sides[0], sides[1] * lax.axis_size("gy"), sides[2] * xs * lax.axis_size("gz"))
    wide = (sides[0], sides[1] + 2 * H, sides[2] + 2 * H)
    images = gather_views(views, sides[2])
    inside = grid_mask(sides, totals)[None]
    taps = psf / jnp.sum(psf, axis=-1, keepdims=True)
    flipped = taps[:, :, ::-1]
    weights = view_weights(extents, sides)
    weight_sum = jnp.sum(weights, axis=0)
    deconvolved = local
    for step in range(ITERS):
        halo = padded(deconvolved, (("gy", 1, 2 * H), (("gx", "gz"), 2, 2 * H)))
        blurred = blur_padded(halo[None], taps, wide)
        ratio = jnp.where(inside, images / blurred, jnp.float32(0.0))
        back = blur_padded(ratio, flipped, sides)
        summed = jnp.sum(weights * back, axis=0)
        deconvolved = deconvolved * (summed / weight_sum)
    return lax.all_to_all(deconvolved, "gx", 0, 2, tiled=True)


def solution(mesh):
    placed = (P(None, "gx", ("gy", "gz"), None), P("gx", "gy", "gz"), P(), P())
    return jax.shard_map(
        shards, mesh=mesh, in_specs=placed, out_specs=P("gx", "gy", "gz"), check_vma=False
    )
```

```python
import jax
import jax.numpy as jnp
from jax import lax
from jax.sharding import PartitionSpec as P

H = 8
K = 17
ITERS = 2


def axis_count(axis):
    names = axis if isinstance(axis, tuple) else (axis,)
    count = 1
    for name in names:
        count *= lax.axis_size(name)
    return count


def padded(array, sides):
    for axis, dim, width in sides:
        devices, length = (axis_count(axis), array.shape[dim])
        rank = list(range(devices))
        if isinstance(axis, tuple):
            inner = lax.axis_size(axis[0])
            rank = [(b % inner) * (devices // inner) + b // inner for b in range(devices)]
        up = [(rank[i], rank[i + 1]) for i in range(devices - 1)]
        down = [(j, i) for i, j in up]
        last = lax.slice_in_dim(array, length - width, length, axis=dim)
        leading = lax.slice_in_dim(array, 0, width, axis=dim)
        before = lax.ppermute(last, axis, up)
        after = lax.ppermute(leading, axis, down)
        array = jnp.concatenate([before, array, after], axis=dim)
    return array


def band_matrix(kernels, length):
    rows = length + 2 * H
    count = kernels.shape[0]
    column = jnp.pad(kernels, ((0, 0), (0, rows + 1 - K)))
    tiled = jnp.tile(column, (1, length))[:, : length * rows]
    return jnp.swapaxes(tiled.reshape(count, length, rows), 1, 2)


def blur_along(padded, kernels, axis, length):
    matrix = band_matrix(kernels, length)
    have = padded.shape[axis]
    low = (length + 2 * H - have) // 2
    matrix = matrix[:, low : low + have]
    source = "vxyz" if padded.shape[0] == kernels.shape[0] else "uxyz"
    letter = "vxyz"[axis]
    target = "vxyz".replace(letter, "a")
    form = source + ",v" + letter + "a->" + target
    return jnp.einsum(form, padded, matrix, precision=lax.Precision.HIGH)


def blur_padded(padded, kernels, sides):
    result = padded
    for axis in range(3):
        result = blur_along(result, kernels[:, axis], axis + 1, sides[axis])
    return result


def positions(sides, margin):
    block = lax.axis_index("gz") * lax.axis_size("gx") + lax.axis_index("gx")
    starts = (0, lax.axis_index("gy") * sides[1], block * sides[2])
    margins = (0, margin, margin)
    return [
        starts[a] - margins[a] + jnp.arange(sides[a] + 2 * margins[a], dtype=jnp.int32)
        for a in range(3)
    ]


def view_weights(extents, sides):
    first, second, third = positions(sides, 0)
    inside_first = (first[None, :] >= extents[:, 0, 0:1]) & (first[None, :] < extents[:, 0, 1:2])
    inside_second = (second[None, :] >= extents[:, 1, 0:1]) & (second[None, :] < extents[:, 1, 1:2])
    inside_third = (third[None, :] >= extents[:, 2, 0:1]) & (third[None, :] < extents[:, 2, 1:2])
    inside = (
        inside_first[:, :, None, None]
        & inside_second[:, None, :, None]
        & inside_third[:, None, None, :]
    )
    return jnp.where(inside, jnp.float32(1.0), jnp.float32(0.25))


def grid_mask(sides, totals):
    first, second, third = positions(sides, H)
    inside = [(p >= 0) & (p < n) for p, n in zip((first, second, third), totals)]
    return inside[0][:, None, None] & inside[1][None, :, None] & inside[2][None, None, :]


def gather_views(views, width):
    xs = lax.axis_size("gx")
    zs = lax.axis_size("gz")
    wide = jnp.pad(views, ((0, 0), (0, 0), (0, 0), (H, H)))
    windows = []
    for gx in range(xs):
        for gz in range(zs):
            start = (gz * xs + gx) * width
            windows.append(lax.slice_in_dim(wide, start, start + width + 2 * H, axis=3))
    sent = jnp.stack(windows)
    got = lax.all_to_all(sent, ("gx", "gz"), 0, 0, tiled=True)
    count, rows, span = views.shape[0], views.shape[2], width + 2 * H
    got = got.reshape(xs, zs, count, views.shape[1], rows, span)
    got = jnp.transpose(got, (2, 0, 3, 1, 4, 5))
    return got.reshape(count, xs * views.shape[1], zs * rows, span)


def shards(views, estimate, psf, extents):
    xs = lax.axis_size("gx")
    local = lax.all_to_all(estimate, "gx", 2, 0, tiled=True)
    sides = local.shape
    totals = (sides[0], sides[1] * lax.axis_size("gy"), sides[2] * xs * lax.axis_size("gz"))
    wide = (sides[0], sides[1] + 2 * H, sides[2] + 2 * H)
    images = gather_views(views, sides[2])
    images = padded(images, (("gy", 2, H),))
    inside = grid_mask(sides, totals)[None]
    taps = psf / jnp.sum(psf, axis=-1, keepdims=True)
    flipped = taps[:, :, ::-1]
    weights = view_weights(extents, sides)
    weight_sum = jnp.sum(weights, axis=0)

    def step(index, deconvolved):
        halo = padded(deconvolved, (("gy", 1, 2 * H), (("gx", "gz"), 2, 2 * H)))
        blurred = blur_padded(halo[None], taps, wide)
        ratio = jnp.where(inside, images / blurred, jnp.float32(0.0))
        back = blur_padded(ratio, flipped, sides)
        summed = jnp.sum(weights * back, axis=0)
        return deconvolved * (summed / weight_sum)

    deconvolved = lax.fori_loop(0, ITERS, step, local)
    return lax.all_to_all(deconvolved, "gx", 0, 2, tiled=True)


def solution(mesh):
    placed = (P(None, "gx", ("gy", "gz"), None), P("gx", "gy", "gz"), P(), P())
    return jax.shard_map(
        shards, mesh=mesh, in_specs=placed, out_specs=P("gx", "gy", "gz"), check_vma=False
    )
```

```python
import jax
import jax.numpy as jnp
from jax import lax
from jax.sharding import PartitionSpec as P

H = 8
K = 17
ITERS = 2


def axis_count(axis):
    names = axis if isinstance(axis, tuple) else (axis,)
    count = 1
    for name in names:
        count *= lax.axis_size(name)
    return count


def padded(array, sides):
    for axis, dim, width in sides:
        devices, length = (axis_count(axis), array.shape[dim])
        rank = list(range(devices))
        if isinstance(axis, tuple):
            inner = lax.axis_size(axis[0])
            rank = [(b % inner) * (devices // inner) + b // inner for b in range(devices)]
        up = [(rank[i], rank[(i + 1) % devices]) for i in range(devices)]
        down = [(j, i) for i, j in up]
        last = lax.slice_in_dim(array, length - width, length, axis=dim)
        leading = lax.slice_in_dim(array, 0, width, axis=dim)
        before = lax.ppermute(last, axis, up)
        after = lax.ppermute(leading, axis, down)
        array = jnp.concatenate([before, array, after], axis=dim)
    return array


def band_matrix(kernels, length):
    rows = length + 2 * H
    count = kernels.shape[0]
    column = jnp.pad(kernels, ((0, 0), (0, rows + 1 - K)))
    tiled = jnp.tile(column, (1, length))[:, : length * rows]
    return jnp.swapaxes(tiled.reshape(count, length, rows), 1, 2)


def blur_along(padded, kernels, axis, length):
    matrix = band_matrix(kernels, length)
    have = padded.shape[axis]
    low = (length + 2 * H - have) // 2
    matrix = matrix[:, low : low + have]
    source = "vxyz" if padded.shape[0] == kernels.shape[0] else "uxyz"
    letter = "vxyz"[axis]
    target = "vxyz".replace(letter, "a")
    form = source + ",v" + letter + "a->" + target
    return jnp.einsum(form, padded, matrix, precision=lax.Precision.HIGH)


def blur_padded(padded, kernels, sides):
    result = padded
    for axis in range(3):
        result = blur_along(result, kernels[:, axis], axis + 1, sides[axis])
    return result


def positions(sides, margin):
    block = lax.axis_index("gz") * lax.axis_size("gx") + lax.axis_index("gx")
    starts = (0, lax.axis_index("gy") * sides[1], block * sides[2])
    margins = (0, margin, margin)
    return [
        starts[a] - margins[a] + jnp.arange(sides[a] + 2 * margins[a], dtype=jnp.int32)
        for a in range(3)
    ]


def view_weights(extents, sides):
    first, second, third = positions(sides, 0)
    inside_first = (first[None, :] >= extents[:, 0, 0:1]) & (first[None, :] < extents[:, 0, 1:2])
    inside_second = (second[None, :] >= extents[:, 1, 0:1]) & (second[None, :] < extents[:, 1, 1:2])
    inside_third = (third[None, :] >= extents[:, 2, 0:1]) & (third[None, :] < extents[:, 2, 1:2])
    inside = (
        inside_first[:, :, None, None]
        & inside_second[:, None, :, None]
        & inside_third[:, None, None, :]
    )
    return jnp.where(inside, jnp.float32(1.0), jnp.float32(0.25))


def grid_mask(sides, totals, margin=H):
    first, second, third = positions(sides, margin)
    inside = [(p >= 0) & (p < n) for p, n in zip((first, second, third), totals)]
    return inside[0][:, None, None] & inside[1][None, :, None] & inside[2][None, None, :]


def gather_views(views, width):
    xs = lax.axis_size("gx")
    zs = lax.axis_size("gz")
    wide = jnp.pad(views, ((0, 0), (0, 0), (0, 0), (H, H)))
    windows = []
    for gx in range(xs):
        for gz in range(zs):
            start = (gz * xs + gx) * width
            windows.append(lax.slice_in_dim(wide, start, start + width + 2 * H, axis=3))
    sent = jnp.stack(windows)
    got = lax.all_to_all(sent, ("gx", "gz"), 0, 0, tiled=True)
    count, rows, span = views.shape[0], views.shape[2], width + 2 * H
    got = got.reshape(xs, zs, count, views.shape[1], rows, span)
    got = jnp.transpose(got, (2, 0, 3, 1, 4, 5))
    return got.reshape(count, xs * views.shape[1], zs * rows, span)


def shards(views, estimate, psf, extents):
    xs = lax.axis_size("gx")
    local = lax.all_to_all(estimate, "gx", 2, 0, tiled=True)
    sides = local.shape
    totals = (sides[0], sides[1] * lax.axis_size("gy"), sides[2] * xs * lax.axis_size("gz"))
    wide = (sides[0], sides[1] + 2 * H, sides[2] + 2 * H)
    images = gather_views(views, sides[2])
    images = padded(images, (("gy", 2, H),))
    inside = grid_mask(sides, totals)[None]
    grid = grid_mask(sides, totals, 2 * H)
    taps = psf / jnp.sum(psf, axis=-1, keepdims=True)
    flipped = taps[:, :, ::-1]
    weights = view_weights(extents, sides)
    weight_sum = jnp.sum(weights, axis=0)
    deconvolved = local
    for step in range(ITERS):
        halo = padded(deconvolved, (("gy", 1, 2 * H), (("gx", "gz"), 2, 2 * H)))
        halo = jnp.where(grid, halo, jnp.float32(0.0))
        blurred = blur_padded(halo[None], taps, wide)
        ratio = jnp.where(inside, images / blurred, jnp.float32(0.0))
        back = blur_padded(ratio, flipped, sides)
        summed = jnp.sum(weights * back, axis=0)
        deconvolved = deconvolved * (summed / weight_sum)
    return lax.all_to_all(deconvolved, "gx", 0, 2, tiled=True)


def solution(mesh):
    placed = (P(None, "gx", ("gy", "gz"), None), P("gx", "gy", "gz"), P(), P())
    return jax.shard_map(
        shards, mesh=mesh, in_specs=placed, out_specs=P("gx", "gy", "gz"), check_vma=False
    )
```

```python
import jax
import jax.numpy as jnp
from jax import lax
from jax.sharding import PartitionSpec as P

H = 8
K = 17
ITERS = 2


def axis_count(axis):
    names = axis if isinstance(axis, tuple) else (axis,)
    count = 1
    for name in names:
        count *= lax.axis_size(name)
    return count


def padded(array, sides):
    for axis, dim, width in sides:
        devices, length = (axis_count(axis), array.shape[dim])
        rank = list(range(devices))
        if isinstance(axis, tuple):
            inner = lax.axis_size(axis[0])
            rank = [(b % inner) * (devices // inner) + b // inner for b in range(devices)]
        up = [(rank[i], rank[i + 1]) for i in range(devices - 1)]
        down = [(j, i) for i, j in up]
        last = lax.slice_in_dim(array, length - width, length, axis=dim)
        leading = lax.slice_in_dim(array, 0, width, axis=dim)
        before = lax.ppermute(last, axis, up)
        after = lax.ppermute(leading, axis, down)
        array = jnp.concatenate([before, array, after], axis=dim)
    return array


def band_matrix(kernels, length):
    rows = length + 2 * H
    count = kernels.shape[0]
    column = jnp.pad(kernels, ((0, 0), (0, rows + 1 - K)))
    tiled = jnp.tile(column, (1, length))[:, : length * rows]
    return jnp.swapaxes(tiled.reshape(count, length, rows), 1, 2)


def blur_along(padded, kernels, axis, length):
    matrix = band_matrix(kernels, length)
    have = padded.shape[axis]
    low = (length + 2 * H - have) // 2
    matrix = matrix[:, low : low + have]
    source = "vxyz" if padded.shape[0] == kernels.shape[0] else "uxyz"
    letter = "vxyz"[axis]
    target = "vxyz".replace(letter, "a")
    form = source + ",v" + letter + "a->" + target
    return jnp.einsum(form, padded, matrix, precision=lax.Precision.HIGH)


def blur_padded(padded, kernels, sides):
    result = padded
    for axis in range(3):
        result = blur_along(result, kernels[:, axis], axis + 1, sides[axis])
    return result


def positions(sides, margin):
    block = lax.axis_index("gz") * lax.axis_size("gx") + lax.axis_index("gx")
    starts = (0, lax.axis_index("gy") * sides[1], block * sides[2])
    margins = (0, margin, margin)
    return [
        starts[a] - margins[a] + jnp.arange(sides[a] + 2 * margins[a], dtype=jnp.int32)
        for a in range(3)
    ]


def view_weights(extents, sides):
    first, second, third = positions(sides, 0)
    inside_first = (first[None, :] >= extents[:, 0, 0:1]) & (first[None, :] < extents[:, 0, 1:2])
    inside_second = (second[None, :] >= extents[:, 1, 0:1]) & (second[None, :] < extents[:, 1, 1:2])
    inside_third = (third[None, :] >= extents[:, 2, 0:1]) & (third[None, :] < extents[:, 2, 1:2])
    inside = (
        inside_first[:, :, None, None]
        & inside_second[:, None, :, None]
        & inside_third[:, None, None, :]
    )
    return jnp.where(inside, jnp.float32(1.0), jnp.float32(0.25))


def grid_mask(sides, totals):
    first, second, third = positions(sides, H)
    inside = [(p >= 0) & (p < n) for p, n in zip((first, second, third), totals)]
    return inside[0][:, None, None] & inside[1][None, :, None] & inside[2][None, None, :]


def gather_views(views, width):
    xs = lax.axis_size("gx")
    zs = lax.axis_size("gz")
    wide = jnp.pad(views, ((0, 0), (0, 0), (0, 0), (H, H)))
    windows = []
    for gx in range(xs):
        for gz in range(zs):
            start = (gz * xs + gx) * width
            windows.append(lax.slice_in_dim(wide, start, start + width + 2 * H, axis=3))
    sent = jnp.stack(windows)
    got = lax.all_to_all(sent, ("gx", "gz"), 0, 0, tiled=True)
    count, rows, span = views.shape[0], views.shape[2], width + 2 * H
    got = got.reshape(xs, zs, count, views.shape[1], rows, span)
    got = jnp.transpose(got, (2, 0, 3, 1, 4, 5))
    return got.reshape(count, xs * views.shape[1], zs * rows, span)


def shards(views, estimate, psf, extents):
    xs = lax.axis_size("gx")
    local = lax.all_to_all(estimate, "gx", 2, 0, tiled=True)
    sides = local.shape
    totals = (sides[0], sides[1] * lax.axis_size("gy"), sides[2] * xs * lax.axis_size("gz"))
    wide = (sides[0], sides[1] + 2 * H, sides[2] + 2 * H)
    images = gather_views(views, sides[2])
    images = padded(images, (("gy", 2, H),))
    inside = grid_mask(sides, totals)[None]
    taps = psf / jnp.sum(psf, axis=-1, keepdims=True)
    flipped = taps[:, :, ::-1]
    weights = view_weights(extents, sides)
    weight_sum = jnp.sum(weights, axis=0)
    deconvolved = local
    for step in range(ITERS):
        halo = padded(deconvolved, ((("gx", "gz"), 2, 2 * H), ("gy", 1, 2 * H)))
        blurred = blur_padded(halo[None], taps, wide)
        ratio = jnp.where(inside, images / blurred, jnp.float32(0.0))
        back = blur_padded(ratio, flipped, sides)
        summed = jnp.sum(weights * back, axis=0)
        deconvolved = deconvolved * (summed / weight_sum)
    return lax.all_to_all(deconvolved, "gx", 0, 2, tiled=True)


def solution(mesh):
    placed = (P(None, "gx", ("gy", "gz"), None), P("gx", "gy", "gz"), P(), P())
    return jax.shard_map(
        shards, mesh=mesh, in_specs=placed, out_specs=P("gx", "gy", "gz"), check_vma=False
    )
```

```python
import jax
import jax.numpy as jnp
from jax import lax
from jax.sharding import PartitionSpec as P

H = 8
K = 17
ITERS = 2


def axis_count(axis):
    names = axis if isinstance(axis, tuple) else (axis,)
    count = 1
    for name in names:
        count *= lax.axis_size(name)
    return count


def padded(array, sides):
    for axis, dim, width in sides:
        devices, length = (axis_count(axis), array.shape[dim])
        rank = list(range(devices))
        if isinstance(axis, tuple):
            inner = lax.axis_size(axis[0])
            rank = [(b % inner) * (devices // inner) + b // inner for b in range(devices)]
        up = [(rank[i], rank[i + 1]) for i in range(devices - 1)]
        down = [(j, i) for i, j in up]
        last = lax.slice_in_dim(array, length - width, length, axis=dim)
        leading = lax.slice_in_dim(array, 0, width, axis=dim)
        before = lax.ppermute(last, axis, up)
        after = lax.ppermute(leading, axis, down)
        array = jnp.concatenate([before, array, after], axis=dim)
    return array


def band_matrix(kernels, length):
    rows = length + 2 * H
    count = kernels.shape[0]
    column = jnp.pad(kernels, ((0, 0), (0, rows + 1 - K)))
    tiled = jnp.tile(column, (1, length))[:, : length * rows]
    return jnp.swapaxes(tiled.reshape(count, length, rows), 1, 2)


def blur_along(padded, kernels, axis, length):
    matrix = band_matrix(kernels, length)
    have = padded.shape[axis]
    low = (length + 2 * H - have) // 2
    matrix = matrix[:, low : low + have]
    source = "vxyz" if padded.shape[0] == kernels.shape[0] else "uxyz"
    letter = "vxyz"[axis]
    target = "vxyz".replace(letter, "a")
    form = source + ",v" + letter + "a->" + target
    return jnp.einsum(form, padded, matrix, precision=lax.Precision.HIGH)


def blur_padded(padded, kernels, sides, order=(0, 1, 2)):
    result = padded
    for axis in order:
        result = blur_along(result, kernels[:, axis], axis + 1, sides[axis])
    return result


def positions(sides, margin):
    block = lax.axis_index("gz") * lax.axis_size("gx") + lax.axis_index("gx")
    starts = (0, lax.axis_index("gy") * sides[1], block * sides[2])
    margins = (0, margin, margin)
    return [
        starts[a] - margins[a] + jnp.arange(sides[a] + 2 * margins[a], dtype=jnp.int32)
        for a in range(3)
    ]


def view_weights(extents, sides):
    first, second, third = positions(sides, 0)
    inside_first = (first[None, :] >= extents[:, 0, 0:1]) & (first[None, :] < extents[:, 0, 1:2])
    inside_second = (second[None, :] >= extents[:, 1, 0:1]) & (second[None, :] < extents[:, 1, 1:2])
    inside_third = (third[None, :] >= extents[:, 2, 0:1]) & (third[None, :] < extents[:, 2, 1:2])
    inside = (
        inside_first[:, :, None, None]
        & inside_second[:, None, :, None]
        & inside_third[:, None, None, :]
    )
    return jnp.where(inside, jnp.float32(1.0), jnp.float32(0.25))


def grid_mask(sides, totals):
    first, second, third = positions(sides, H)
    inside = [(p >= 0) & (p < n) for p, n in zip((first, second, third), totals)]
    return inside[0][:, None, None] & inside[1][None, :, None] & inside[2][None, None, :]


def gather_views(views, width):
    xs = lax.axis_size("gx")
    zs = lax.axis_size("gz")
    wide = jnp.pad(views, ((0, 0), (0, 0), (0, 0), (H, H)))
    windows = []
    for gx in range(xs):
        for gz in range(zs):
            start = (gz * xs + gx) * width
            windows.append(lax.slice_in_dim(wide, start, start + width + 2 * H, axis=3))
    sent = jnp.stack(windows)
    got = lax.all_to_all(sent, ("gx", "gz"), 0, 0, tiled=True)
    count, rows, span = views.shape[0], views.shape[2], width + 2 * H
    got = got.reshape(xs, zs, count, views.shape[1], rows, span)
    got = jnp.transpose(got, (2, 0, 3, 1, 4, 5))
    return got.reshape(count, xs * views.shape[1], zs * rows, span)


def shards(views, estimate, psf, extents):
    xs = lax.axis_size("gx")
    local = lax.all_to_all(estimate, "gx", 2, 0, tiled=True)
    sides = local.shape
    totals = (sides[0], sides[1] * lax.axis_size("gy"), sides[2] * xs * lax.axis_size("gz"))
    wide = (sides[0], sides[1] + 2 * H, sides[2] + 2 * H)
    images = gather_views(views, sides[2])
    images = padded(images, (("gy", 2, H),))
    inside = grid_mask(sides, totals)[None]
    taps = psf / jnp.sum(psf, axis=-1, keepdims=True)
    flipped = taps[:, :, ::-1]
    weights = view_weights(extents, sides)
    weight_sum = jnp.sum(weights, axis=0)
    deconvolved = local
    for step in range(ITERS):
        halo = padded(deconvolved, ((("gx", "gz"), 2, 2 * H), ("gy", 1, 2 * H)))
        blurred = blur_padded(halo[None], taps, wide, (1, 2, 0))
        ratio = jnp.where(inside, images / blurred, jnp.float32(0.0))
        back = blur_padded(ratio, flipped, sides)
        summed = jnp.sum(weights * back, axis=0)
        deconvolved = deconvolved * (summed / weight_sum)
    return lax.all_to_all(deconvolved, "gx", 0, 2, tiled=True)


def solution(mesh):
    placed = (P(None, "gx", ("gy", "gz"), None), P("gx", "gy", "gz"), P(), P())
    return jax.shard_map(
        shards, mesh=mesh, in_specs=placed, out_specs=P("gx", "gy", "gz"), check_vma=False
    )
```

```python
import jax
import jax.numpy as jnp
from jax import lax
from jax.sharding import PartitionSpec as P

H = 8
K = 17
ITERS = 2


def axis_count(axis):
    names = axis if isinstance(axis, tuple) else (axis,)
    count = 1
    for name in names:
        count *= lax.axis_size(name)
    return count


def padded(array, sides):
    for axis, dim, width in sides:
        devices, length = (axis_count(axis), array.shape[dim])
        rank = list(range(devices))
        if isinstance(axis, tuple):
            inner = lax.axis_size(axis[0])
            rank = [(b % inner) * (devices // inner) + b // inner for b in range(devices)]
        up = [(rank[i], rank[i + 1]) for i in range(devices - 1)]
        down = [(j, i) for i, j in up]
        last = lax.slice_in_dim(array, length - width, length, axis=dim)
        leading = lax.slice_in_dim(array, 0, width, axis=dim)
        before = lax.ppermute(last, axis, up)
        after = lax.ppermute(leading, axis, down)
        array = jnp.concatenate([before, array, after], axis=dim)
    return array


def band_matrix(kernels, length):
    rows = length + 2 * H
    count = kernels.shape[0]
    column = jnp.pad(kernels, ((0, 0), (0, rows + 1 - K)))
    tiled = jnp.tile(column, (1, length))[:, : length * rows]
    return jnp.swapaxes(tiled.reshape(count, length, rows), 1, 2)


def blur_along(padded, kernels, axis, length):
    matrix = band_matrix(kernels, length)
    have = padded.shape[axis]
    low = (length + 2 * H - have) // 2
    matrix = matrix[:, low : low + have]
    source = "vxyz" if padded.shape[0] == kernels.shape[0] else "uxyz"
    letter = "vxyz"[axis]
    target = "vxyz".replace(letter, "a")
    form = source + ",v" + letter + "a->" + target
    return jnp.einsum(form, padded, matrix, precision=lax.Precision.HIGH)


def blur_padded(padded, kernels, sides, order=(0, 1, 2)):
    result = padded
    for axis in order:
        result = blur_along(result, kernels[:, axis], axis + 1, sides[axis])
    return result


def positions(sides, margin):
    block = lax.axis_index("gz") * lax.axis_size("gx") + lax.axis_index("gx")
    starts = (0, lax.axis_index("gy") * sides[1], block * sides[2])
    margins = (0, margin, margin)
    return [
        starts[a] - margins[a] + jnp.arange(sides[a] + 2 * margins[a], dtype=jnp.int32)
        for a in range(3)
    ]


def view_weights(extents, sides):
    first, second, third = positions(sides, 0)
    inside_first = (first[None, :] >= extents[:, 0, 0:1]) & (first[None, :] < extents[:, 0, 1:2])
    inside_second = (second[None, :] >= extents[:, 1, 0:1]) & (second[None, :] < extents[:, 1, 1:2])
    inside_third = (third[None, :] >= extents[:, 2, 0:1]) & (third[None, :] < extents[:, 2, 1:2])
    inside = (
        inside_first[:, :, None, None]
        & inside_second[:, None, :, None]
        & inside_third[:, None, None, :]
    )
    return jnp.where(inside, jnp.float32(1.0), jnp.float32(0.25))


def grid_mask(sides, totals):
    first, second, third = positions(sides, H)
    inside = [(p >= 0) & (p < n) for p, n in zip((first, second, third), totals)]
    return inside[0][:, None, None] & inside[1][None, :, None] & inside[2][None, None, :]


def gather_views(views, width):
    xs = lax.axis_size("gx")
    zs = lax.axis_size("gz")
    wide = jnp.pad(views, ((0, 0), (0, 0), (0, 0), (H, H)))
    windows = []
    for gx in range(xs):
        for gz in range(zs):
            start = (gz * xs + gx) * width
            windows.append(lax.slice_in_dim(wide, start, start + width + 2 * H, axis=3))
    sent = jnp.stack(windows)
    got = lax.all_to_all(sent, ("gx", "gz"), 0, 0, tiled=True)
    count, rows, span = views.shape[0], views.shape[2], width + 2 * H
    got = got.reshape(xs, zs, count, views.shape[1], rows, span)
    got = jnp.transpose(got, (2, 0, 3, 1, 4, 5))
    return got.reshape(count, xs * views.shape[1], zs * rows, span)


def shards(views, estimate, psf, extents):
    xs = lax.axis_size("gx")
    local = lax.all_to_all(estimate, "gx", 2, 0, tiled=True)
    sides = local.shape
    totals = (sides[0], sides[1] * lax.axis_size("gy"), sides[2] * xs * lax.axis_size("gz"))
    wide = (sides[0], sides[1] + 2 * H, sides[2] + 2 * H)
    images = gather_views(views, sides[2])
    images = padded(images, (("gy", 2, H),))
    inside = grid_mask(sides, totals)[None]
    taps = psf / jnp.sum(psf, axis=-1, keepdims=True)
    flipped = taps[:, :, ::-1]
    weights = view_weights(extents, sides)
    weight_sum = jnp.sum(weights, axis=0)
    deconvolved = local
    for step in range(ITERS):
        halo = padded(deconvolved, ((("gx", "gz"), 2, 2 * H), ("gy", 1, 2 * H)))
        blurred = blur_padded(halo[None], taps, wide, (1, 2, 0))
        ratio = jnp.where(inside, images / blurred, jnp.float32(0.0))
        back = blur_padded(ratio, flipped, sides, (1, 2, 0))
        summed = jnp.sum(weights * back, axis=0)
        deconvolved = deconvolved * (summed / weight_sum)
    return lax.all_to_all(deconvolved, "gx", 0, 2, tiled=True)


def solution(mesh):
    placed = (P(None, "gx", ("gy", "gz"), None), P("gx", "gy", "gz"), P(), P())
    return jax.shard_map(
        shards, mesh=mesh, in_specs=placed, out_specs=P("gx", "gy", "gz"), check_vma=False
    )
```
